256 devices in a mesh: dom: 16 (over z, core), grp: 16 (over y, x).
Axes of the slice: x: 4, y: 4, z: 8, core: 2. Of those that a mesh axis runs over, the one named last changes fastest.
Arguments:
- positions: float32 [65536, 3, 128], P(('dom', 'grp')), may hold values from -4 to 4
- velocities: float32 [65536, 3, 128], P(('dom', 'grp')), may hold values from -9 to 9
- masses: float32 [65536, 128], P(('dom', 'grp')), may hold values from 0.3 to 3
- destination: int32 [65536], P(('dom', 'grp')), may hold values from 0 to 15, as said below
- group_ids: int32 [65536, 128], P(('dom', 'grp')), may hold values from 0 to 1023, as said below
- boundary_set: int32 [256, 64], P(('dom', 'grp')), may hold values from 0 to 511, as said below
- send_list: int32 [256, 16, 16], P(('dom', 'grp')), may hold values from 0 to 63, as said below
- send_count: int32 [256, 16], P(('dom', 'grp')), may hold values from 0 to 16, as said below
- partners: int32 [131072, 4], P(('dom', 'grp')), may hold values from 0 to 767, as said below
Outputs:
- energy: float32 [65536, 128], P(('dom', 'grp'))
- group_kinetic: float32 [1024], replicated
The draws below stay inside these ranges and needn't reach their ends.
Inputs may be any that keep to these rules, and one draw needn't show every extreme that they name: Each block of 256 leaves sends at most 32 leaves to one destination; in each dom index one destination receives exactly 32 leaves from every block. `group_ids`: the particles of block b carry the 16 group numbers 4 * b to 4 * b + 15, taken modulo 1024, each at least once and no others. `boundary_set`: each row holds 64 distinct slot numbers. `send_list`: each row of 16 holds distinct positions. `send_count`: A block sends nothing to its own grp index; in each dom index one grp index receives 16 from every other block. `partners`: each row holds 4 distinct entry numbers of combined.
All inputs are finite; a program needn't handle non-finite values.
Results may differ from the reference program's by a relative error of at most 0.0003.
Values sent between devices are 32-bit elements; how exact they have to be, the bound alone decides.
No kernel may reach another device: no remote copies, remote signals or barrier semaphores. Data moves between devices by JAX's collectives and lax.ppermute only.
A program may use at most 64 MiB of HBM per device.

```python
import math
import jax
import jax.numpy as jnp
from jax import lax

LEAF = 128
LEAF_IN = 256
PAIRS = 4
GSPAN = 16
GROUP_DEV = 4
DOMAINS = 16
COOWN = 16
CAP = 32
SLOTS = 512
BSET = 64
B_PEER = 16
GROUPS = 1024
LEAVES = 65536
N_DOM = 16
N_GRP = 16


def routing(key):
    base = jax.random.fold_in(key, 11)
    block_total = DOMAINS * COOWN
    full_owner = jax.random.randint(jax.random.fold_in(base, 1), (DOMAINS,), 0, COOWN)
    pool_size = (COOWN - 1) * CAP
    remaining = LEAF_IN - CAP
    pool_range = jnp.arange(pool_size, dtype=jnp.int32)

    def one_block(block_index):
        block_key = jax.random.fold_in(base, 100 + block_index)
        favoured = full_owner[block_index // COOWN]
        jitter = jax.random.randint(jax.random.fold_in(block_key, 1), (pool_size,), 0, 4096)
        priority = ((pool_range == 0) | (pool_range == (COOWN - 2) * CAP)).astype(jnp.int32)
        scores = jitter * pool_size + pool_range + priority * (4096 * pool_size)
        picked = lax.top_k(scores, remaining)[1]
        others = picked // CAP
        leaf_dest = others + (others >= favoured).astype(jnp.int32)
        assigned = jnp.concatenate([jnp.full((CAP,), favoured, jnp.int32), leaf_dest.astype(jnp.int32)])
        shuffle = jax.random.permutation(jax.random.fold_in(block_key, 2), LEAF_IN)
        return assigned[shuffle]
    return (jax.vmap(one_block)(jnp.arange(block_total, dtype=jnp.int32)), full_owner)


def slot_live(assigned):
    block_total = DOMAINS * COOWN
    counts = jnp.sum((assigned[:, :, None] == jnp.arange(COOWN, dtype=jnp.int32)[None, None, :]).astype(jnp.int32), axis=1)
    per_owner = jnp.transpose(counts.reshape(DOMAINS, COOWN, COOWN), (0, 2, 1)).reshape(block_total, COOWN)
    usable = jnp.arange(CAP, dtype=jnp.int32)[None, None, :] < per_owner[:, :, None]
    return usable.reshape(block_total, SLOTS).astype(jnp.int32)


def peer_lists(key):
    base = jax.random.fold_in(key, 31)
    block_total = DOMAINS * COOWN
    full_peer = jax.random.randint(jax.random.fold_in(base, 1), (DOMAINS,), 0, COOWN - 1)
    peer_of = full_peer[jnp.arange(block_total, dtype=jnp.int32) // COOWN]
    source_index = jnp.arange(block_total, dtype=jnp.int32) % COOWN
    dest_range = jnp.arange(COOWN, dtype=jnp.int32)
    set_range = jnp.arange(BSET, dtype=jnp.int32)
    jitter = jax.random.randint(jax.random.fold_in(base, 2), (block_total, COOWN, BSET), 0, 4096)
    last_first = (dest_range[None, :, None] == peer_of[:, None, None]) & (set_range[None, None, :] == BSET - 1)
    zero_first = (dest_range[None, :, None] == (peer_of[:, None, None] + 1) % COOWN) & (set_range[None, None, :] == 0)
    scores = jitter * BSET + set_range[None, None, :] + (last_first | zero_first).astype(jnp.int32) * (4096 * BSET)
    set_lists = lax.top_k(scores, B_PEER)[1].astype(jnp.int32)
    counts = jax.random.randint(jax.random.fold_in(base, 3), (block_total, COOWN), 0, B_PEER + 1)
    counts = jnp.where(dest_range[None, :] == peer_of[:, None], B_PEER, counts)
    counts = jnp.where(dest_range[None, :] == source_index[:, None], 0, counts)
    return (set_lists, counts.astype(jnp.int32))


def group_offsets(key):
    block_total = DOMAINS * COOWN
    per_block = LEAF_IN * LEAF
    offsets = jax.random.randint(jax.random.fold_in(key, 51), (block_total, per_block), 0, GSPAN)
    return offsets.at[:, :GSPAN].set(jnp.arange(GSPAN, dtype=jnp.int32)[None, :])


def pick_rows(drift_table, offset_row):
    return drift_table[offset_row]


def draw_destination(key, part):
    assigned, full_owner = routing(key)
    return assigned.reshape(-1).astype(jnp.int32)


def draw_group_ids(key, part):
    block_total = DOMAINS * COOWN
    offsets = group_offsets(key)
    labels = (jnp.arange(block_total, dtype=jnp.int32)[:, None] * GROUP_DEV + offsets) % GROUPS
    return labels.reshape(block_total * LEAF_IN, LEAF).astype(jnp.int32)


def draw_velocities(key, part):
    block_total = DOMAINS * COOWN
    per_block = LEAF_IN * LEAF
    offsets = group_offsets(key)
    drifts = jax.random.truncated_normal(jax.random.fold_in(key, 61), -3.0, 3.0, (block_total, GSPAN, 3))
    particle_drift = jax.vmap(pick_rows)(drifts, offsets)
    spread = jax.random.truncated_normal(jax.random.fold_in(key, 62), -3.0, 3.0, (block_total, per_block, 3))
    values = 1.5 * particle_drift + spread
    values = values.reshape(block_total * LEAF_IN, LEAF, 3)
    return jnp.transpose(values, (0, 2, 1)).astype(jnp.float32)


def draw_boundary_set(key, part):
    block_total = DOMAINS * COOWN
    assigned, full_owner = routing(key)
    slot_ok = slot_live(assigned)
    slot_range = jnp.arange(SLOTS, dtype=jnp.int32)
    jitter = jax.random.randint(jax.random.fold_in(key, 23), (block_total, SLOTS), 0, 4096)
    block_range = jnp.arange(block_total, dtype=jnp.int32)
    is_full = (block_range % COOWN == full_owner[block_range // COOWN]).astype(jnp.int32)
    extremes = ((slot_range == 0) | (slot_range == SLOTS - 1)).astype(jnp.int32)
    scores = jitter * SLOTS + slot_range[None, :] + slot_ok * (2 * 4096 * SLOTS)
    scores = scores + is_full[:, None] * extremes[None, :] * (4 * 4096 * SLOTS)
    return lax.top_k(scores, BSET)[1].astype(jnp.int32)


def draw_send_list(key, part):
    set_lists, counts = peer_lists(key)
    return set_lists


def draw_send_count(key, part):
    set_lists, counts = peer_lists(key)
    return counts


def draw_partners(key, part):
    block_total = DOMAINS * COOWN
    assigned, full_owner = routing(key)
    slot_ok = slot_live(assigned)
    set_lists, counts = peer_lists(key)
    per_owner = jnp.transpose(counts.reshape(DOMAINS, COOWN, COOWN), (0, 2, 1)).reshape(block_total, COOWN)
    remote_ok = (jnp.arange(B_PEER, dtype=jnp.int32)[None, None, :] < per_owner[:, :, None]).reshape(block_total, COOWN * B_PEER)
    table_ok = jnp.concatenate([slot_ok, remote_ok.astype(jnp.int32)], axis=1)
    table_size = SLOTS + COOWN * B_PEER
    table_range = jnp.arange(table_size, dtype=jnp.int32)
    base = jax.random.fold_in(key, 41)
    first_row = (jnp.arange(SLOTS, dtype=jnp.int32) == 0).astype(jnp.int32)
    extremes = ((table_range == 0) | (table_range == table_size - 1)).astype(jnp.int32)

    def one_owner(inputs):
        owner_index, usable = inputs
        jitter = jax.random.randint(jax.random.fold_in(base, owner_index), (SLOTS, table_size), 0, 2048)
        scores = jitter * table_size + table_range[None, :] + usable[None, :] * (2 * 2048 * table_size)
        scores = scores + first_row[:, None] * (extremes * usable)[None, :] * (4 * 2048 * table_size)
        return lax.top_k(scores, PAIRS)[1].astype(jnp.int32)
    chosen = lax.map(one_owner, (jnp.arange(block_total, dtype=jnp.int32), table_ok))
    return chosen.reshape(block_total * SLOTS, PAIRS)


def steps_of(stream_key, extent, cuts, low, high):
    def one(position, parts):
        steps = jax.random.uniform(jax.random.fold_in(jax.random.fold_in(stream_key, 6), position), (parts,), jnp.float32, low / len(cuts), high / len(cuts))
        return jnp.repeat(jnp.exp(steps), extent[position] // parts).reshape((-1,) + (1,) * (len(extent) - position - 1))

    loudness = one(*cuts[0])
    for cut in cuts[1:]:
        loudness = loudness * one(*cut)
    return loudness


def centred(stream_key, dims, deviation, bound, shards=(), held_as=jnp.bfloat16):
    values = deviation * jax.random.normal(stream_key, dims, jnp.float32)
    if shards:
        values = values * steps_of(stream_key, dims, shards, -0.22, 0.18)
    return jnp.clip(values, -bound, bound).astype(held_as)


def setup_inputs(seed: int = 0) -> dict:
    seeds = jax.random.split(jax.random.key(seed), 10)
    positions = centred(seeds[0], (LEAVES, 3, LEAF), 1.0, 4.0, ((0, 256),), jnp.float32)
    velocities = draw_velocities(jax.random.fold_in(seeds[9], 71), 0)
    masses = jnp.clip(jnp.exp(math.log(3.0) - 2.3025851 * jax.random.uniform(seeds[2], (LEAVES, LEAF), jnp.float32) ** steps_of(seeds[2], (LEAVES, LEAF), ((0, 256),), -0.2, 0.2)), 0.3, 3.0)
    destination = draw_destination(jax.random.fold_in(seeds[9], 71), 0)
    group_ids = draw_group_ids(jax.random.fold_in(seeds[9], 71), 0)
    boundary_set = draw_boundary_set(jax.random.fold_in(seeds[9], 71), 0)
    send_list = draw_send_list(jax.random.fold_in(seeds[9], 71), 0)
    send_count = draw_send_count(jax.random.fold_in(seeds[9], 71), 0)
    partners = draw_partners(jax.random.fold_in(seeds[9], 71), 0)
    return {"positions": positions, "velocities": velocities, "masses": masses, "destination": destination, "group_ids": group_ids, "boundary_set": boundary_set, "send_list": send_list, "send_count": send_count, "partners": partners}


softening = 0.0025

def tile_potential(targets, sources):
    distance = softening
    for component in range(3):
        offset = targets[:, None, component, :, None] - sources[:, :, component, None, :]
        distance = distance + offset * offset
    weights = sources[:, :, 3, None, :] * lax.rsqrt(distance)
    return -lax.optimization_barrier(jnp.sum(weights, axis=(1, 3)))

def slot_potential(owned, combined, pair_index, coupling):
    slot_count = owned.shape[0]
    leaf_width = owned.shape[2]
    block_rows = max(32, slot_count // 16)

    def one_block(inputs):
        targets, indices = inputs
        sources = jnp.take(combined, indices, axis=0)
        return tile_potential(targets, sources)
    result = lax.map(one_block, (owned.reshape(slot_count // block_rows, block_rows, 4, leaf_width), pair_index.reshape(slot_count // block_rows, block_rows, pair_index.shape[1])))
    return result.reshape(slot_count, leaf_width) * coupling

def reference(positions, velocities, masses, destination, group_ids, boundary_set, send_list, send_count, partners):
    block_total = N_DOM * N_GRP
    mass_flat = masses.reshape(-1)
    group_flat = group_ids.reshape(-1)
    mass_total = jax.ops.segment_sum(mass_flat, group_flat, num_segments=GROUPS)
    kinetic = jnp.zeros_like(mass_flat)
    for component in range(3):
        speed = velocities[:, component, :].reshape(-1)
        bulk_velocity = jax.ops.segment_sum(mass_flat * speed, group_flat, num_segments=GROUPS) / mass_total
        relative = speed - bulk_velocity[group_flat]
        kinetic = kinetic + relative * relative
    kinetic = 0.5 * kinetic
    group_kinetic = jax.ops.segment_sum(mass_flat * kinetic, group_flat, num_segments=GROUPS) / mass_total
    leaf_dest = destination.reshape(block_total, LEAF_IN)
    onehot = (leaf_dest[:, :, None] == jnp.arange(COOWN, dtype=jnp.int32)[None, None, :]).astype(jnp.int32)
    leaf_rank = lax.optimization_barrier(jnp.sum((jnp.cumsum(onehot, axis=1) - onehot) * onehot, axis=2))
    block_range = jnp.arange(block_total, dtype=jnp.int32)
    source = block_range % COOWN
    owner_block = (block_range // COOWN)[:, None] * COOWN + leaf_dest
    where_slot = (owner_block * SLOTS + source[:, None] * CAP + leaf_rank).astype(jnp.int32)
    payload = jnp.concatenate([positions, masses[:, None, :]], axis=1)
    tables = jnp.zeros((block_total * SLOTS, 4, LEAF), positions.dtype).at[where_slot.reshape(-1)].set(payload)
    tables = tables.reshape(block_total, SLOTS, 4, LEAF)
    coupling = 1.0 / (PAIRS * LEAF)
    source_rows = jnp.arange(COOWN, dtype=jnp.int32)

    def owner_potential(block_index):
        domain = block_index // COOWN
        grp_index = block_index % COOWN
        row_tables = lax.dynamic_slice_in_dim(tables, domain * COOWN, COOWN, 0)
        owned = lax.dynamic_index_in_dim(row_tables, grp_index, 0, keepdims=False)
        senders = domain * COOWN + source_rows
        peer_list = send_list[senders, grp_index]
        slot_pick = jnp.take_along_axis(boundary_set[senders], peer_list, axis=1)
        remote = row_tables[source_rows[:, None], slot_pick]
        is_live = jnp.arange(B_PEER, dtype=jnp.int32)[None, :] < send_count[senders, grp_index][:, None]
        remote = jnp.where(is_live[:, :, None, None], remote, jnp.zeros_like(remote))
        combined = jnp.concatenate([owned, remote.reshape(COOWN * B_PEER, 4, LEAF)], axis=0)
        pair_index = lax.dynamic_slice_in_dim(partners, block_index * SLOTS, SLOTS, 0)
        return slot_potential(owned, combined, pair_index, coupling)
    potential = lax.map(owner_potential, block_range)
    own_potential = potential.reshape(block_total * SLOTS, LEAF)[where_slot.reshape(-1)]
    energy = kinetic.reshape(block_total * LEAF_IN, LEAF) + own_potential
    return (energy, group_kinetic)
```

```python
import jax
import jax.numpy as jnp
from jax import lax
from jax.sharding import PartitionSpec as P

GSPAN = 16
GROUP_DEV = 4


softening = 0.0025
exact = lax.Precision.HIGHEST


def tile_potential(targets, sources):
    distance = softening
    for component in range(3):
        offset = targets[:, None, component, :, None] - sources[:, :, component, None, :]
        distance = distance + offset * offset
    weights = sources[:, :, 3, None, :] * lax.rsqrt(distance)
    return -jnp.sum(weights, axis=(1, 3))


def group_totals(gathered):
    blocks, stats, span = gathered.shape
    split = gathered.reshape(blocks, stats, span // GROUP_DEV, GROUP_DEV)
    total = split[:, :, 0, :]
    for shift in range(1, span // GROUP_DEV):
        total = total + jnp.roll(split[:, :, shift, :], shift, axis=0)
    return jnp.transpose(total, (1, 0, 2)).reshape(stats, blocks * GROUP_DEV)


def shards(
    positions,
    velocities,
    masses,
    destination,
    group_ids,
    boundary_set,
    send_list,
    send_count,
    partners,
):
    owners = lax.axis_size("grp")
    leaves = positions.shape[0]
    leaf_width = positions.shape[2]
    capacity = 2 * leaves // owners
    slot_count = owners * capacity
    groups = GROUP_DEV * lax.axis_size("dom") * owners
    block_index = lax.axis_index("dom") * owners + lax.axis_index("grp")
    first_group = block_index * GROUP_DEV
    mass_flat = masses.reshape(-1)
    group_flat = group_ids.reshape(-1)
    speeds = jnp.transpose(velocities, (1, 0, 2)).reshape(3, -1)
    local_ids = (group_flat - first_group) % groups
    member = (jnp.arange(GSPAN, dtype=jnp.int32)[:, None] == local_ids[None, :]).astype(jnp.float32)

    def local_sums(stats):
        return jnp.einsum(
            "kp,gp->kg", stats, member, precision=exact, preferred_element_type=jnp.float32
        )

    def near_groups(table):
        doubled = jnp.concatenate([table, table[:, :GSPAN]], axis=1)
        return lax.dynamic_slice_in_dim(doubled, first_group, GSPAN, axis=1)

    first_sums = local_sums(jnp.concatenate([mass_flat[None, :], mass_flat[None, :] * speeds], axis=0))
    every_first = lax.all_gather(first_sums, ("dom", "grp"), axis=0, tiled=False)
    totals = group_totals(every_first)
    mass_total = totals[0]
    near = near_groups(totals)
    bulk_local = near[1:] / near[0:1]
    per_particle = jnp.dot(bulk_local, member, precision=exact, preferred_element_type=jnp.float32)
    relative = speeds - per_particle
    kinetic = 0.5 * jnp.sum(relative * relative, axis=0)
    heat_local = local_sums((mass_flat * kinetic)[None, :])
    every_heat = lax.all_gather(heat_local, ("dom", "grp"), axis=0, tiled=False)
    heat_sum = group_totals(every_heat)[0]
    group_kinetic = heat_sum / mass_total

    onehot = (destination[:, None] == jnp.arange(owners, dtype=jnp.int32)[None, :]).astype(jnp.int32)
    leaf_rank = jnp.sum((jnp.cumsum(onehot, axis=0) - onehot) * onehot, axis=1)
    target = destination * capacity + leaf_rank
    payload = jnp.concatenate([positions, masses[:, None, :]], axis=1)
    placing = (jnp.arange(slot_count, dtype=jnp.int32)[:, None] == target[None, :]).astype(jnp.float32)
    outgoing = jnp.dot(
        placing, payload.reshape(leaves, -1), precision=exact, preferred_element_type=jnp.float32
    ).reshape(slot_count, 4, leaf_width)
    owned = lax.all_to_all(outgoing, "grp", split_axis=0, concat_axis=0, tiled=True)

    per_peer = send_list.shape[2]
    pick = jnp.take(boundary_set[0], send_list[0], axis=0)
    live = jnp.arange(per_peer, dtype=jnp.int32)[None, :] < send_count[0][:, None]
    sending = jnp.take(owned, pick, axis=0)
    sending = jnp.where(live[:, :, None, None], sending, jnp.zeros_like(sending))
    remote = lax.all_to_all(sending, "grp", split_axis=0, concat_axis=0, tiled=True)
    remote = remote.reshape(owners * per_peer, 4, leaf_width)
    combined = jnp.concatenate([owned, remote], axis=0)

    coupling = 1.0 / (partners.shape[1] * leaf_width)
    sources = jnp.take(combined, partners, axis=0)
    potential = tile_potential(owned, sources) * coupling
    returned = lax.all_to_all(potential, "grp", split_axis=0, concat_axis=0, tiled=True)
    own_potential = jnp.take(returned, target, axis=0)
    energy = kinetic.reshape(leaves, leaf_width) + own_potential
    return (energy, group_kinetic)


def solution(mesh):
    in_specs = (
        P(("dom", "grp"), None, None),
        P(("dom", "grp"), None, None),
        P(("dom", "grp"), None),
        P(("dom", "grp")),
        P(("dom", "grp"), None),
        P(("dom", "grp"), None),
        P(("dom", "grp"), None, None),
        P(("dom", "grp"), None),
        P(("dom", "grp"), None),
    )
    out_specs = (P(("dom", "grp"), None), P())
    return jax.shard_map(shards, mesh=mesh, in_specs=in_specs, out_specs=out_specs, check_vma=False)
```

```python
import jax
import jax.numpy as jnp
from jax import lax
from jax.sharding import PartitionSpec as P

GSPAN = 16
GROUP_DEV = 4


softening = 0.0025
exact = lax.Precision.HIGHEST


def tile_potential(targets, sources):
    distance = softening
    for component in range(3):
        offset = targets[:, None, component, :, None] - sources[:, :, component, None, :]
        distance = distance + offset * offset
    weights = sources[:, :, 3, None, :] * lax.rsqrt(distance)
    return -jnp.sum(weights, axis=(1, 3))


def shards(
    positions,
    velocities,
    masses,
    destination,
    group_ids,
    boundary_set,
    send_list,
    send_count,
    partners,
):
    owners = lax.axis_size("grp")
    leaves = positions.shape[0]
    leaf_width = positions.shape[2]
    capacity = 2 * leaves // owners
    slot_count = owners * capacity
    groups = GROUP_DEV * lax.axis_size("dom") * owners
    block_index = lax.axis_index("dom") * owners + lax.axis_index("grp")
    first_group = block_index * GROUP_DEV
    mass_flat = masses.reshape(-1)
    group_flat = group_ids.reshape(-1)
    speeds = jnp.transpose(velocities, (1, 0, 2)).reshape(3, -1)
    local_ids = (group_flat - first_group) % groups
    member = (jnp.arange(GSPAN, dtype=jnp.int32)[:, None] == local_ids[None, :]).astype(jnp.float32)

    def local_sums(stats):
        return jnp.einsum(
            "kp,gp->kg", stats, member, precision=exact, preferred_element_type=jnp.float32
        )

    blocks = lax.axis_size("dom") * owners
    quarters = GSPAN // GROUP_DEV

    def from_block(value, step):
        if step == 0:
            return value
        ring = [(i, (i - step) % blocks) for i in range(blocks)]
        return lax.ppermute(value, ("dom", "grp"), ring)

    first_sums = local_sums(jnp.concatenate([mass_flat[None, :], mass_flat[None, :] * speeds], axis=0))
    near_sums = {step: from_block(first_sums, step) for step in range(-quarters + 1, quarters)}
    near_parts = []
    for ahead in range(quarters):
        part = 0.0
        for back in range(quarters):
            part = part + near_sums[ahead - back][:, back * GROUP_DEV:(back + 1) * GROUP_DEV]
        near_parts.append(part)
    near = jnp.concatenate(near_parts, axis=1)
    bulk_local = near[1:] / near[0:1]
    per_particle = jnp.dot(bulk_local, member, precision=exact, preferred_element_type=jnp.float32)
    relative = speeds - per_particle
    kinetic = 0.5 * jnp.sum(relative * relative, axis=0)
    heat_local = local_sums((mass_flat * kinetic)[None, :])[0]
    heat_own = heat_local[:GROUP_DEV]
    for back in range(1, quarters):
        heat_own = heat_own + from_block(heat_local[back * GROUP_DEV:(back + 1) * GROUP_DEV], -back)
    kinetic_own = heat_own / near[0, :GROUP_DEV]
    across = jnp.broadcast_to(kinetic_own[None, :], (owners, GROUP_DEV))
    across = lax.all_to_all(across, "grp", split_axis=0, concat_axis=0, tiled=True)
    domains = lax.axis_size("dom")
    every = jnp.broadcast_to(across[None], (domains, owners, GROUP_DEV))
    every = lax.all_to_all(every, "dom", split_axis=0, concat_axis=0, tiled=True)
    group_kinetic = every.reshape(groups)

    onehot = (destination[:, None] == jnp.arange(owners, dtype=jnp.int32)[None, :]).astype(jnp.int32)
    leaf_rank = jnp.sum((jnp.cumsum(onehot, axis=0) - onehot) * onehot, axis=1)
    target = destination * capacity + leaf_rank
    payload = jnp.concatenate([positions, masses[:, None, :]], axis=1)
    placing = (jnp.arange(slot_count, dtype=jnp.int32)[:, None] == target[None, :]).astype(jnp.float32)
    outgoing = jnp.dot(
        placing, payload.reshape(leaves, -1), precision=exact, preferred_element_type=jnp.float32
    ).reshape(slot_count, 4, leaf_width)
    owned = lax.all_to_all(outgoing, "grp", split_axis=0, concat_axis=0, tiled=True)

    per_peer = send_list.shape[2]
    pick = jnp.take(boundary_set[0], send_list[0], axis=0)
    live = jnp.arange(per_peer, dtype=jnp.int32)[None, :] < send_count[0][:, None]
    sending = jnp.take(owned, pick, axis=0)
    sending = jnp.where(live[:, :, None, None], sending, jnp.zeros_like(sending))
    remote = lax.all_to_all(sending, "grp", split_axis=0, concat_axis=0, tiled=True)
    remote = remote.reshape(owners * per_peer, 4, leaf_width)
    combined = jnp.concatenate([owned, remote], axis=0)

    coupling = 1.0 / (partners.shape[1] * leaf_width)
    sources = jnp.take(combined, partners, axis=0)
    potential = tile_potential(owned, sources) * coupling
    returned = lax.all_to_all(potential, "grp", split_axis=0, concat_axis=0, tiled=True)
    own_potential = jnp.take(returned, target, axis=0)
    energy = kinetic.reshape(leaves, leaf_width) + own_potential
    return (energy, group_kinetic)


def solution(mesh):
    in_specs = (
        P(("dom", "grp"), None, None),
        P(("dom", "grp"), None, None),
        P(("dom", "grp"), None),
        P(("dom", "grp")),
        P(("dom", "grp"), None),
        P(("dom", "grp"), None),
        P(("dom", "grp"), None, None),
        P(("dom", "grp"), None),
        P(("dom", "grp"), None),
    )
    out_specs = (P(("dom", "grp"), None), P())
    return jax.shard_map(shards, mesh=mesh, in_specs=in_specs, out_specs=out_specs, check_vma=False)
```

```python
import jax
import jax.numpy as jnp
from jax import lax
from jax.sharding import PartitionSpec as P

GSPAN = 16
GROUP_DEV = 4


softening = 0.0025
exact = lax.Precision.HIGHEST


def tile_potential(targets, sources):
    distance = softening
    for component in range(3):
        offset = targets[:, None, component, :, None] - sources[:, :, component, None, :]
        distance = distance + offset * offset
    weights = sources[:, :, 3, None, :] * lax.rsqrt(distance)
    return -jnp.sum(weights, axis=(1, 3))


def shards(
    positions,
    velocities,
    masses,
    destination,
    group_ids,
    boundary_set,
    send_list,
    send_count,
    partners,
):
    owners = lax.axis_size("grp")
    leaves = positions.shape[0]
    leaf_width = positions.shape[2]
    capacity = 2 * leaves // owners
    slot_count = owners * capacity
    groups = GROUP_DEV * lax.axis_size("dom") * owners
    block_index = lax.axis_index("dom") * owners + lax.axis_index("grp")
    first_group = block_index * GROUP_DEV
    mass_flat = masses.reshape(-1)
    group_flat = group_ids.reshape(-1)
    speeds = jnp.transpose(velocities, (1, 0, 2)).reshape(3, -1)
    local_ids = (group_flat - first_group) % groups
    member = (jnp.arange(GSPAN, dtype=jnp.int32)[:, None] == local_ids[None, :]).astype(jnp.float32)

    def local_sums(stats):
        return jnp.einsum(
            "kp,gp->kg", stats, member, precision=exact, preferred_element_type=jnp.float32
        )

    onehot = (destination[:, None] == jnp.arange(owners, dtype=jnp.int32)[None, :]).astype(jnp.int32)
    leaf_rank = jnp.sum((jnp.cumsum(onehot, axis=0) - onehot) * onehot, axis=1)
    target = destination * capacity + leaf_rank
    payload = jnp.concatenate([positions, masses[:, None, :]], axis=1)
    placing = (jnp.arange(slot_count, dtype=jnp.int32)[:, None] == target[None, :]).astype(jnp.float32)
    outgoing = jnp.dot(
        placing, payload.reshape(leaves, -1), precision=exact, preferred_element_type=jnp.float32
    ).reshape(slot_count, 4, leaf_width)
    owned = lax.all_to_all(outgoing, "grp", split_axis=0, concat_axis=0, tiled=True)

    per_peer = send_list.shape[2]
    pick = boundary_set[0].at[send_list[0]].get(mode="promise_in_bounds")
    live = jnp.arange(per_peer, dtype=jnp.int32)[None, :] < send_count[0][:, None]
    sending = owned.at[pick].get(mode="promise_in_bounds")
    sending = jnp.where(live[:, :, None, None], sending, jnp.zeros_like(sending))
    remote = lax.all_to_all(sending, "grp", split_axis=0, concat_axis=0, tiled=True)
    remote = remote.reshape(owners * per_peer, 4, leaf_width)
    combined = jnp.concatenate([owned, remote], axis=0)

    blocks = lax.axis_size("dom") * owners
    quarters = GSPAN // GROUP_DEV

    def from_block(value, step):
        if step == 0:
            return value
        ring = [(i, (i - step) % blocks) for i in range(blocks)]
        return lax.ppermute(value, ("dom", "grp"), ring)

    first_sums = local_sums(jnp.concatenate([mass_flat[None, :], mass_flat[None, :] * speeds], axis=0))
    first_sums, remote = lax.optimization_barrier((first_sums, remote))
    near_sums = {step: from_block(first_sums, step) for step in range(-quarters + 1, quarters)}
    near_parts = []
    for ahead in range(quarters):
        part = 0.0
        for back in range(quarters):
            part = part + near_sums[ahead - back][:, back * GROUP_DEV:(back + 1) * GROUP_DEV]
        near_parts.append(part)
    near = jnp.concatenate(near_parts, axis=1)
    bulk_local = near[1:] / near[0:1]
    per_particle = jnp.dot(bulk_local, member, precision=exact, preferred_element_type=jnp.float32)
    relative = speeds - per_particle
    kinetic = 0.5 * jnp.sum(relative * relative, axis=0)
    heat_local = local_sums((mass_flat * kinetic)[None, :])[0]
    heat_own = heat_local[:GROUP_DEV]
    for back in range(1, quarters):
        heat_own = heat_own + from_block(heat_local[back * GROUP_DEV:(back + 1) * GROUP_DEV], -back)
    kinetic_own = heat_own / near[0, :GROUP_DEV]
    across = jnp.broadcast_to(kinetic_own[None, :], (owners, GROUP_DEV))
    across = lax.all_to_all(across, "grp", split_axis=0, concat_axis=0, tiled=True)
    domains = lax.axis_size("dom")
    every = jnp.broadcast_to(across[None], (domains, owners, GROUP_DEV))
    every = lax.all_to_all(every, "dom", split_axis=0, concat_axis=0, tiled=True)
    group_kinetic = every.reshape(groups)

    coupling = 1.0 / (partners.shape[1] * leaf_width)
    sources = combined.at[partners].get(mode="promise_in_bounds")
    potential = tile_potential(owned, sources) * coupling
    returned = lax.all_to_all(potential, "grp", split_axis=0, concat_axis=0, tiled=True)
    own_potential = returned.at[target].get(mode="promise_in_bounds")
    energy = kinetic.reshape(leaves, leaf_width) + own_potential
    return (energy, group_kinetic)


def solution(mesh):
    in_specs = (
        P(("dom", "grp"), None, None),
        P(("dom", "grp"), None, None),
        P(("dom", "grp"), None),
        P(("dom", "grp")),
        P(("dom", "grp"), None),
        P(("dom", "grp"), None),
        P(("dom", "grp"), None, None),
        P(("dom", "grp"), None),
        P(("dom", "grp"), None),
    )
    out_specs = (P(("dom", "grp"), None), P())
    return jax.shard_map(shards, mesh=mesh, in_specs=in_specs, out_specs=out_specs, check_vma=False)
```

```python
import jax
import jax.numpy as jnp
from jax import lax
from jax.sharding import PartitionSpec as P
from jax.experimental import pallas as pl
from jax.experimental.pallas import tpu as pltpu

GSPAN = 16
GROUP_DEV = 4


softening = 0.0025
exact = lax.Precision.HIGHEST


def tile_potential(targets, sources):
    distance = softening
    for component in range(3):
        offset = targets[:, None, component, :, None] - sources[:, :, component, None, :]
        distance = distance + offset * offset
    weights = sources[:, :, 3, None, :] * lax.rsqrt(distance)
    return -jnp.sum(weights, axis=(1, 3))


def pair_kernel(index_ref, table_ref, out_ref, acc_ref, *, rows, pairs, coupling):
    width = table_ref.shape[2]
    ones = jnp.ones((8, width), jnp.float32)
    first = pl.program_id(0) * rows

    def one_slot(t, carry):
        slot = first + t
        target = table_ref[slot]
        columns = jnp.transpose(jnp.concatenate([target, jnp.zeros_like(target)], axis=0))
        picked = [table_ref[index_ref[slot * pairs + p]] for p in range(pairs)]
        for c in range(width // 8):
            tx = columns[8 * c:8 * c + 8, 0:1]
            ty = columns[8 * c:8 * c + 8, 1:2]
            tz = columns[8 * c:8 * c + 8, 2:3]
            acc = jnp.zeros((8, width), jnp.float32)
            for src in picked:
                dx = tx - src[0:1, :]
                dy = ty - src[1:2, :]
                dz = tz - src[2:3, :]
                distance = softening + dx * dx
                distance = distance + dy * dy
                distance = distance + dz * dz
                acc = acc + src[3:4, :] * lax.rsqrt(distance)
            acc_ref[8 * c:8 * c + 8, :] = acc
        total = lax.dot_general(
            ones, acc_ref[...], (((1,), (1,)), ((), ())), precision=exact,
            preferred_element_type=jnp.float32,
        )
        out_ref[pl.ds(t, 1), :] = -total[0:1, :] * coupling
        return carry

    lax.fori_loop(0, rows, one_slot, 0)


def slot_potential(combined, partners, slot_count, coupling):
    rows = 8
    width = combined.shape[2]
    pairs = partners.shape[1]
    grid_spec = pltpu.PrefetchScalarGridSpec(
        num_scalar_prefetch=1,
        grid=(slot_count // rows,),
        in_specs=[pl.BlockSpec(combined.shape, lambda i, index: (0, 0, 0))],
        out_specs=pl.BlockSpec((rows, width), lambda i, index: (i, 0)),
        scratch_shapes=[pltpu.VMEM((width, width), jnp.float32)],
    )
    body = lambda *refs: pair_kernel(*refs, rows=rows, pairs=pairs, coupling=coupling)
    return pl.pallas_call(
        body,
        grid_spec=grid_spec,
        out_shape=jax.ShapeDtypeStruct((slot_count, width), jnp.float32),
    )(partners.reshape(-1), combined)


def shards(
    positions,
    velocities,
    masses,
    destination,
    group_ids,
    boundary_set,
    send_list,
    send_count,
    partners,
):
    owners = lax.axis_size("grp")
    leaves = positions.shape[0]
    leaf_width = positions.shape[2]
    capacity = 2 * leaves // owners
    slot_count = owners * capacity
    groups = GROUP_DEV * lax.axis_size("dom") * owners
    block_index = lax.axis_index("dom") * owners + lax.axis_index("grp")
    first_group = block_index * GROUP_DEV
    mass_flat = masses.reshape(-1)
    group_flat = group_ids.reshape(-1)
    speeds = jnp.transpose(velocities, (1, 0, 2)).reshape(3, -1)
    local_ids = (group_flat - first_group) % groups
    member = (jnp.arange(GSPAN, dtype=jnp.int32)[:, None] == local_ids[None, :]).astype(jnp.float32)

    def local_sums(stats):
        return jnp.einsum(
            "kp,gp->kg", stats, member, precision=exact, preferred_element_type=jnp.float32
        )

    onehot = (destination[:, None] == jnp.arange(owners, dtype=jnp.int32)[None, :]).astype(jnp.int32)
    leaf_rank = jnp.sum((jnp.cumsum(onehot, axis=0) - onehot) * onehot, axis=1)
    target = destination * capacity + leaf_rank
    payload = jnp.concatenate([positions, masses[:, None, :]], axis=1)
    placing = (jnp.arange(slot_count, dtype=jnp.int32)[:, None] == target[None, :]).astype(jnp.float32)
    outgoing = jnp.dot(
        placing, payload.reshape(leaves, -1), precision=exact, preferred_element_type=jnp.float32
    ).reshape(slot_count, 4, leaf_width)
    owned = lax.all_to_all(outgoing, "grp", split_axis=0, concat_axis=0, tiled=True)

    per_peer = send_list.shape[2]
    pick = boundary_set[0].at[send_list[0]].get(mode="promise_in_bounds")
    live = jnp.arange(per_peer, dtype=jnp.int32)[None, :] < send_count[0][:, None]
    sending = owned.at[pick].get(mode="promise_in_bounds")
    sending = jnp.where(live[:, :, None, None], sending, jnp.zeros_like(sending))
    remote = lax.all_to_all(sending, "grp", split_axis=0, concat_axis=0, tiled=True)
    remote = remote.reshape(owners * per_peer, 4, leaf_width)
    combined = jnp.concatenate([owned, remote], axis=0)

    blocks = lax.axis_size("dom") * owners
    quarters = GSPAN // GROUP_DEV

    def from_block(value, step):
        if step == 0:
            return value
        ring = [(i, (i - step) % blocks) for i in range(blocks)]
        return lax.ppermute(value, ("dom", "grp"), ring)

    first_sums = local_sums(jnp.concatenate([mass_flat[None, :], mass_flat[None, :] * speeds], axis=0))
    first_sums, remote = lax.optimization_barrier((first_sums, remote))
    near_sums = {step: from_block(first_sums, step) for step in range(-quarters + 1, quarters)}
    near_parts = []
    for ahead in range(quarters):
        part = 0.0
        for back in range(quarters):
            part = part + near_sums[ahead - back][:, back * GROUP_DEV:(back + 1) * GROUP_DEV]
        near_parts.append(part)
    near = jnp.concatenate(near_parts, axis=1)
    bulk_local = near[1:] / near[0:1]
    per_particle = jnp.dot(bulk_local, member, precision=exact, preferred_element_type=jnp.float32)
    relative = speeds - per_particle
    kinetic = 0.5 * jnp.sum(relative * relative, axis=0)
    heat_local = local_sums((mass_flat * kinetic)[None, :])[0]
    heat_own = heat_local[:GROUP_DEV]
    for back in range(1, quarters):
        heat_own = heat_own + from_block(heat_local[back * GROUP_DEV:(back + 1) * GROUP_DEV], -back)
    kinetic_own = heat_own / near[0, :GROUP_DEV]
    across = jnp.broadcast_to(kinetic_own[None, :], (owners, GROUP_DEV))
    across = lax.all_to_all(across, "grp", split_axis=0, concat_axis=0, tiled=True)
    domains = lax.axis_size("dom")
    every = jnp.broadcast_to(across[None], (domains, owners, GROUP_DEV))
    every = lax.all_to_all(every, "dom", split_axis=0, concat_axis=0, tiled=True)
    group_kinetic = every.reshape(groups)

    coupling = 1.0 / (partners.shape[1] * leaf_width)
    potential = slot_potential(combined, partners, slot_count, coupling)
    returned = lax.all_to_all(potential, "grp", split_axis=0, concat_axis=0, tiled=True)
    own_potential = returned.at[target].get(mode="promise_in_bounds")
    energy = kinetic.reshape(leaves, leaf_width) + own_potential
    return (energy, group_kinetic)


def solution(mesh):
    in_specs = (
        P(("dom", "grp"), None, None),
        P(("dom", "grp"), None, None),
        P(("dom", "grp"), None),
        P(("dom", "grp")),
        P(("dom", "grp"), None),
        P(("dom", "grp"), None),
        P(("dom", "grp"), None, None),
        P(("dom", "grp"), None),
        P(("dom", "grp"), None),
    )
    out_specs = (P(("dom", "grp"), None), P())
    return jax.shard_map(shards, mesh=mesh, in_specs=in_specs, out_specs=out_specs, check_vma=False)
```

```python
import jax
import jax.numpy as jnp
from jax import lax
from jax.sharding import PartitionSpec as P

GSPAN = 16
GROUP_DEV = 4


softening = 0.0025
exact = lax.Precision.HIGHEST


def tile_potential(targets, sources):
    distance = softening
    for component in range(3):
        offset = targets[:, None, component, :, None] - sources[:, :, component, None, :]
        distance = distance + offset * offset
    weights = sources[:, :, 3, None, :] * lax.rsqrt(distance)
    return -jnp.sum(weights, axis=(1, 3))


def shards(
    positions,
    velocities,
    masses,
    destination,
    group_ids,
    boundary_set,
    send_list,
    send_count,
    partners,
):
    owners = lax.axis_size("grp")
    leaves = positions.shape[0]
    leaf_width = positions.shape[2]
    capacity = 2 * leaves // owners
    slot_count = owners * capacity
    groups = GROUP_DEV * lax.axis_size("dom") * owners
    block_index = lax.axis_index("dom") * owners + lax.axis_index("grp")
    first_group = block_index * GROUP_DEV
    mass_flat = masses.reshape(-1)
    group_flat = group_ids.reshape(-1)
    speeds = jnp.transpose(velocities, (1, 0, 2)).reshape(3, -1)
    local_ids = (group_flat - first_group) % groups
    member = (jnp.arange(GSPAN, dtype=jnp.int32)[:, None] == local_ids[None, :]).astype(jnp.float32)

    def local_sums(stats):
        return jnp.einsum(
            "kp,gp->kg", stats, member, precision=exact, preferred_element_type=jnp.float32
        )

    onehot = (destination[:, None] == jnp.arange(owners, dtype=jnp.int32)[None, :]).astype(jnp.int32)
    leaf_rank = jnp.sum((jnp.cumsum(onehot, axis=0) - onehot) * onehot, axis=1)
    target = destination * capacity + leaf_rank
    payload = jnp.concatenate([positions, masses[:, None, :]], axis=1)
    placing = (jnp.arange(slot_count, dtype=jnp.int32)[:, None] == target[None, :]).astype(jnp.float32)
    outgoing = jnp.dot(
        placing, payload.reshape(leaves, -1), precision=exact, preferred_element_type=jnp.float32
    ).reshape(slot_count, 4, leaf_width)
    owned = lax.all_to_all(outgoing, "grp", split_axis=0, concat_axis=0, tiled=True)

    per_peer = send_list.shape[2]
    pick = boundary_set[0].at[send_list[0]].get(mode="promise_in_bounds")
    live = jnp.arange(per_peer, dtype=jnp.int32)[None, :] < send_count[0][:, None]
    sending = owned.at[pick].get(mode="promise_in_bounds")
    sending = jnp.where(live[:, :, None, None], sending, jnp.zeros_like(sending))
    remote = lax.all_to_all(sending, "grp", split_axis=0, concat_axis=0, tiled=True)
    remote = remote.reshape(owners * per_peer, 4, leaf_width)
    combined = jnp.concatenate([owned, remote], axis=0)

    blocks = lax.axis_size("dom") * owners
    quarters = GSPAN // GROUP_DEV

    def from_block(value, step):
        if step == 0:
            return value
        ring = [(i, (i - step) % blocks) for i in range(blocks)]
        return lax.ppermute(value, ("dom", "grp"), ring)

    first_sums = local_sums(jnp.concatenate([mass_flat[None, :], mass_flat[None, :] * speeds], axis=0))
    first_sums, remote = lax.optimization_barrier((first_sums, remote))
    near_sums = {step: from_block(first_sums, step) for step in range(-quarters + 1, quarters)}
    near_parts = []
    for ahead in range(quarters):
        part = 0.0
        for back in range(quarters):
            part = part + near_sums[ahead - back][:, back * GROUP_DEV:(back + 1) * GROUP_DEV]
        near_parts.append(part)
    near = jnp.concatenate(near_parts, axis=1)
    bulk_local = near[1:] / near[0:1]
    per_particle = jnp.dot(bulk_local, member, precision=exact, preferred_element_type=jnp.float32)
    relative = speeds - per_particle
    kinetic = 0.5 * jnp.sum(relative * relative, axis=0)
    heat_local = local_sums((mass_flat * kinetic)[None, :])[0]
    partial = jnp.stack([heat_local, first_sums[0]])
    across = jnp.broadcast_to(partial[None], (owners,) + partial.shape)
    across = lax.all_to_all(across, "grp", split_axis=0, concat_axis=0, tiled=True)
    domains = lax.axis_size("dom")
    every = jnp.broadcast_to(across[None], (domains,) + across.shape)
    every = lax.all_to_all(every, "dom", split_axis=0, concat_axis=0, tiled=True)
    every = every.reshape(blocks, 2, quarters, GROUP_DEV)
    totals = every[:, :, 0, :]
    for back in range(1, quarters):
        totals = totals + jnp.roll(every[:, :, back, :], back, axis=0)
    group_kinetic = totals[:, 0, :].reshape(groups) / totals[:, 1, :].reshape(groups)

    coupling = 1.0 / (partners.shape[1] * leaf_width)
    halves = []
    half = slot_count // 2
    for part in range(2):
        rows = partners[part * half:(part + 1) * half]
        sources = combined.at[rows].get(mode="promise_in_bounds")
        halves.append(tile_potential(owned[part * half:(part + 1) * half], sources))
    potential = jnp.concatenate(halves, axis=0) * coupling
    returned = lax.all_to_all(potential, "grp", split_axis=0, concat_axis=0, tiled=True)
    own_potential = returned.at[target].get(mode="promise_in_bounds")
    energy = kinetic.reshape(leaves, leaf_width) + own_potential
    return (energy, group_kinetic)


def solution(mesh):
    in_specs = (
        P(("dom", "grp"), None, None),
        P(("dom", "grp"), None, None),
        P(("dom", "grp"), None),
        P(("dom", "grp")),
        P(("dom", "grp"), None),
        P(("dom", "grp"), None),
        P(("dom", "grp"), None, None),
        P(("dom", "grp"), None),
        P(("dom", "grp"), None),
    )
    out_specs = (P(("dom", "grp"), None), P())
    return jax.shard_map(shards, mesh=mesh, in_specs=in_specs, out_specs=out_specs, check_vma=False)
```

```python
import jax
import jax.numpy as jnp
from jax import lax
from jax.sharding import PartitionSpec as P

GSPAN = 16
GROUP_DEV = 4


softening = 0.0025
exact = lax.Precision.HIGHEST


def tile_potential(targets, sources):
    distance = softening
    for component in range(3):
        offset = targets[:, None, component, :, None] - sources[:, :, component, None, :]
        distance = distance + offset * offset
    weights = sources[:, :, 3, None, :] * lax.rsqrt(distance)
    return -jnp.sum(weights, axis=(1, 3))


def shards(
    positions,
    velocities,
    masses,
    destination,
    group_ids,
    boundary_set,
    send_list,
    send_count,
    partners,
):
    owners = lax.axis_size("grp")
    leaves = positions.shape[0]
    leaf_width = positions.shape[2]
    capacity = 2 * leaves // owners
    slot_count = owners * capacity
    groups = GROUP_DEV * lax.axis_size("dom") * owners
    block_index = lax.axis_index("dom") * owners + lax.axis_index("grp")
    first_group = block_index * GROUP_DEV
    mass_flat = masses.reshape(-1)
    group_flat = group_ids.reshape(-1)
    speeds = jnp.transpose(velocities, (1, 0, 2)).reshape(3, -1)
    local_ids = (group_flat - first_group) % groups
    member = (jnp.arange(GSPAN, dtype=jnp.int32)[:, None] == local_ids[None, :]).astype(jnp.float32)

    def local_sums(stats):
        return jnp.einsum(
            "kp,gp->kg", stats, member, precision=exact, preferred_element_type=jnp.float32
        )

    onehot = (destination[:, None] == jnp.arange(owners, dtype=jnp.int32)[None, :]).astype(jnp.int32)
    leaf_rank = jnp.sum((jnp.cumsum(onehot, axis=0) - onehot) * onehot, axis=1)
    target = destination * capacity + leaf_rank
    payload = jnp.concatenate([positions, masses[:, None, :]], axis=1)
    placing = (jnp.arange(slot_count, dtype=jnp.int32)[:, None] == target[None, :]).astype(jnp.float32)
    outgoing = jnp.dot(
        placing, payload.reshape(leaves, -1), precision=exact, preferred_element_type=jnp.float32
    ).reshape(slot_count, 4, leaf_width)
    owned = lax.all_to_all(outgoing, "grp", split_axis=0, concat_axis=0, tiled=True)

    per_peer = send_list.shape[2]
    pick = boundary_set[0].at[send_list[0]].get(mode="promise_in_bounds")
    live = jnp.arange(per_peer, dtype=jnp.int32)[None, :] < send_count[0][:, None]
    sending = owned.at[pick].get(mode="promise_in_bounds")
    sending = jnp.where(live[:, :, None, None], sending, jnp.zeros_like(sending))
    blocks = lax.axis_size("dom") * owners
    quarters = GSPAN // GROUP_DEV
    first_sums = local_sums(jnp.concatenate([mass_flat[None, :], mass_flat[None, :] * speeds], axis=0))
    leaf_size = per_peer * 4 * leaf_width
    packed = jnp.concatenate(
        [sending.reshape(owners, leaf_size), jnp.broadcast_to(first_sums.reshape(1, -1), (owners, first_sums.size))],
        axis=1,
    )
    packed = lax.all_to_all(packed, "grp", split_axis=0, concat_axis=0, tiled=True)
    remote = packed[:, :leaf_size].reshape(owners * per_peer, 4, leaf_width)
    row_sums = packed[:, leaf_size:].reshape((owners,) + first_sums.shape)
    domains = lax.axis_size("dom")
    before = lax.ppermute(row_sums, "dom", [(i, (i + 1) % domains) for i in range(domains)])
    after = lax.ppermute(row_sums, "dom", [(i, (i - 1) % domains) for i in range(domains)])
    three_rows = jnp.concatenate([before, row_sums, after], axis=0)
    span = 2 * quarters - 1
    window = lax.dynamic_slice_in_dim(three_rows, owners + lax.axis_index("grp") - (quarters - 1), span, axis=0)
    near_sums = {step: window[step + quarters - 1] for step in range(-quarters + 1, quarters)}
    combined = jnp.concatenate([owned, remote], axis=0)

    near_parts = []
    for ahead in range(quarters):
        part = 0.0
        for back in range(quarters):
            part = part + near_sums[ahead - back][:, back * GROUP_DEV:(back + 1) * GROUP_DEV]
        near_parts.append(part)
    near = jnp.concatenate(near_parts, axis=1)
    bulk_local = near[1:] / near[0:1]
    per_particle = jnp.dot(bulk_local, member, precision=exact, preferred_element_type=jnp.float32)
    relative = speeds - per_particle
    kinetic = 0.5 * jnp.sum(relative * relative, axis=0)
    heat_local = local_sums((mass_flat * kinetic)[None, :])[0]
    partial = jnp.stack([heat_local, first_sums[0]])
    across = jnp.broadcast_to(partial[None], (owners,) + partial.shape)
    across = lax.all_to_all(across, "grp", split_axis=0, concat_axis=0, tiled=True)
    every = jnp.broadcast_to(across[None], (domains,) + across.shape)
    every = lax.all_to_all(every, "dom", split_axis=0, concat_axis=0, tiled=True)
    every = every.reshape(blocks, 2, quarters, GROUP_DEV)
    totals = every[:, :, 0, :]
    for back in range(1, quarters):
        totals = totals + jnp.roll(every[:, :, back, :], back, axis=0)
    group_kinetic = totals[:, 0, :].reshape(groups) / totals[:, 1, :].reshape(groups)

    coupling = 1.0 / (partners.shape[1] * leaf_width)
    halves = []
    half = slot_count // 2
    for part in range(2):
        rows = partners[part * half:(part + 1) * half]
        sources = combined.at[rows].get(mode="promise_in_bounds")
        halves.append(tile_potential(owned[part * half:(part + 1) * half], sources))
    potential = jnp.concatenate(halves, axis=0) * coupling
    returned = lax.all_to_all(potential, "grp", split_axis=0, concat_axis=0, tiled=True)
    own_potential = returned.at[target].get(mode="promise_in_bounds")
    energy = kinetic.reshape(leaves, leaf_width) + own_potential
    return (energy, group_kinetic)


def solution(mesh):
    in_specs = (
        P(("dom", "grp"), None, None),
        P(("dom", "grp"), None, None),
        P(("dom", "grp"), None),
        P(("dom", "grp")),
        P(("dom", "grp"), None),
        P(("dom", "grp"), None),
        P(("dom", "grp"), None, None),
        P(("dom", "grp"), None),
        P(("dom", "grp"), None),
    )
    out_specs = (P(("dom", "grp"), None), P())
    return jax.shard_map(shards, mesh=mesh, in_specs=in_specs, out_specs=out_specs, check_vma=False)
```

```python
import jax
import jax.numpy as jnp
from jax import lax
from jax.sharding import PartitionSpec as P

GSPAN = 16
GROUP_DEV = 4


softening = 0.0025
exact = lax.Precision.HIGHEST


def tile_potential(targets, sources):
    distance = softening
    for component in range(3):
        offset = targets[:, None, component, :, None] - sources[:, :, component, None, :]
        distance = distance + offset * offset
    weights = sources[:, :, 3, None, :] * lax.rsqrt(distance)
    return -jnp.sum(weights, axis=(1, 3))


def layer(
    positions,
    velocities,
    masses,
    destination,
    group_ids,
    boundary_set,
    send_list,
    send_count,
    partners,
):
    owners = lax.axis_size("grp")
    leaves = positions.shape[0]
    leaf_width = positions.shape[2]
    capacity = 2 * leaves // owners
    slot_count = owners * capacity
    groups = GROUP_DEV * lax.axis_size("dom") * owners
    block_index = lax.axis_index("dom") * owners + lax.axis_index("grp")
    first_group = block_index * GROUP_DEV
    mass_flat = masses.reshape(-1)
    group_flat = group_ids.reshape(-1)
    speeds = jnp.transpose(velocities, (1, 0, 2)).reshape(3, -1)
    local_ids = (group_flat - first_group) % groups
    member = (jnp.arange(GSPAN, dtype=jnp.int32)[:, None] == local_ids[None, :]).astype(jnp.float32)

    def local_sums(stats):
        return jnp.einsum(
            "kp,gp->kg", stats, member, precision=exact, preferred_element_type=jnp.float32
        )

    onehot = (destination[:, None] == jnp.arange(owners, dtype=jnp.int32)[None, :]).astype(jnp.int32)
    leaf_rank = jnp.sum((jnp.cumsum(onehot, axis=0) - onehot) * onehot, axis=1)
    target = destination * capacity + leaf_rank
    payload = jnp.concatenate([positions, masses[:, None, :]], axis=1)
    placing = (jnp.arange(slot_count, dtype=jnp.int32)[:, None] == target[None, :]).astype(jnp.float32)
    outgoing = jnp.dot(
        placing, payload.reshape(leaves, -1), precision=exact, preferred_element_type=jnp.float32
    ).reshape(slot_count, 4, leaf_width)
    owned = lax.all_to_all(outgoing, "grp", split_axis=0, concat_axis=0, tiled=True)

    per_peer = send_list.shape[2]
    pick = boundary_set[0].at[send_list[0]].get(mode="promise_in_bounds")
    live = jnp.arange(per_peer, dtype=jnp.int32)[None, :] < send_count[0][:, None]
    sending = owned.at[pick].get(mode="promise_in_bounds")
    sending = jnp.where(live[:, :, None, None], sending, jnp.zeros_like(sending))
    blocks = lax.axis_size("dom") * owners
    quarters = GSPAN // GROUP_DEV
    first_sums = local_sums(jnp.concatenate([mass_flat[None, :], mass_flat[None, :] * speeds], axis=0))
    leaf_size = per_peer * 4 * leaf_width
    packed = jnp.concatenate(
        [sending.reshape(owners, leaf_size), jnp.broadcast_to(first_sums.reshape(1, -1), (owners, first_sums.size))],
        axis=1,
    )
    packed = lax.all_to_all(packed, "grp", split_axis=0, concat_axis=0, tiled=True)
    remote = packed[:, :leaf_size].reshape(owners * per_peer, 4, leaf_width)
    row_sums = packed[:, leaf_size:].reshape((owners,) + first_sums.shape)
    domains = lax.axis_size("dom")
    before = lax.ppermute(row_sums, "dom", [(i, (i + 1) % domains) for i in range(domains)])
    after = lax.ppermute(row_sums, "dom", [(i, (i - 1) % domains) for i in range(domains)])
    three_rows = jnp.concatenate([before, row_sums, after], axis=0)
    span = 2 * quarters - 1
    window = lax.dynamic_slice_in_dim(three_rows, owners + lax.axis_index("grp") - (quarters - 1), span, axis=0)
    near_sums = {step: window[step + quarters - 1] for step in range(-quarters + 1, quarters)}
    combined = jnp.concatenate([owned, remote], axis=0)

    near_parts = []
    for ahead in range(quarters):
        part = 0.0
        for back in range(quarters):
            part = part + near_sums[ahead - back][:, back * GROUP_DEV:(back + 1) * GROUP_DEV]
        near_parts.append(part)
    near = jnp.concatenate(near_parts, axis=1)
    bulk_local = near[1:] / near[0:1]
    per_particle = jnp.dot(bulk_local, member, precision=exact, preferred_element_type=jnp.float32)
    relative = speeds - per_particle
    kinetic = 0.5 * jnp.sum(relative * relative, axis=0)
    heat_local = local_sums((mass_flat * kinetic)[None, :])[0]
    partial = jnp.stack([heat_local, first_sums[0]])
    down = jnp.broadcast_to(partial[None], (domains,) + partial.shape)
    down = lax.all_to_all(down, "dom", split_axis=0, concat_axis=0, tiled=True)

    coupling = 1.0 / (partners.shape[1] * leaf_width)
    halves = []
    half = slot_count // 2
    for part in range(2):
        rows = partners[part * half:(part + 1) * half]
        sources = combined.at[rows].get(mode="promise_in_bounds")
        halves.append(tile_potential(owned[part * half:(part + 1) * half], sources))
    potential = jnp.concatenate(halves, axis=0) * coupling
    flat = potential.reshape(owners, capacity * leaf_width)
    extra = jnp.broadcast_to(down.reshape(1, -1), (owners, down.size))
    back = lax.all_to_all(jnp.concatenate([flat, extra], axis=1), "grp", split_axis=0, concat_axis=0, tiled=True)
    returned = back[:, :capacity * leaf_width].reshape(slot_count, leaf_width)
    every = back[:, capacity * leaf_width:].reshape((owners, domains) + partial.shape)
    every = jnp.transpose(every, (1, 0, 2, 3)).reshape(blocks, 2, quarters, GROUP_DEV)
    totals = every[:, :, 0, :]
    for shift in range(1, quarters):
        totals = totals + jnp.roll(every[:, :, shift, :], shift, axis=0)
    group_kinetic = totals[:, 0, :].reshape(groups) / totals[:, 1, :].reshape(groups)
    own_potential = returned.at[target].get(mode="promise_in_bounds")
    energy = kinetic.reshape(leaves, leaf_width) + own_potential
    return (energy, group_kinetic)


def solution(mesh):
    in_specs = (
        P(("dom", "grp"), None, None),
        P(("dom", "grp"), None, None),
        P(("dom", "grp"), None),
        P(("dom", "grp")),
        P(("dom", "grp"), None),
        P(("dom", "grp"), None),
        P(("dom", "grp"), None, None),
        P(("dom", "grp"), None),
        P(("dom", "grp"), None),
    )
    out_specs = (P(("dom", "grp"), None), P())
    return jax.shard_map(layer, mesh=mesh, in_specs=in_specs, out_specs=out_specs, check_vma=False)
```

```python
import jax
import jax.numpy as jnp
from jax import lax
from jax.sharding import PartitionSpec as P

GSPAN = 16
GROUP_DEV = 4


softening = 0.0025
exact = lax.Precision.HIGHEST


def tile_potential(targets, sources):
    distance = softening
    for component in range(3):
        offset = targets[:, None, component, :, None] - sources[:, :, component, None, :]
        distance = distance + offset * offset
    weights = sources[:, :, 3, None, :] * lax.rsqrt(distance)
    return -jnp.sum(weights, axis=(1, 3))


def layer(
    positions,
    velocities,
    masses,
    destination,
    group_ids,
    boundary_set,
    send_list,
    send_count,
    partners,
):
    owners = lax.axis_size("grp")
    leaves = positions.shape[0]
    leaf_width = positions.shape[2]
    capacity = 2 * leaves // owners
    slot_count = owners * capacity
    groups = GROUP_DEV * lax.axis_size("dom") * owners
    block_index = lax.axis_index("dom") * owners + lax.axis_index("grp")
    first_group = block_index * GROUP_DEV
    mass_flat = masses.reshape(-1)
    group_flat = group_ids.reshape(-1)
    speeds = jnp.transpose(velocities, (1, 0, 2)).reshape(3, -1)
    local_ids = (group_flat - first_group) % groups
    member = (jnp.arange(GSPAN, dtype=jnp.int32)[:, None] == local_ids[None, :]).astype(jnp.float32)

    def local_sums(stats):
        return jnp.einsum(
            "kp,gp->kg", stats, member, precision=exact, preferred_element_type=jnp.float32
        )

    onehot = (destination[:, None] == jnp.arange(owners, dtype=jnp.int32)[None, :]).astype(jnp.int32)
    leaf_rank = jnp.sum((jnp.cumsum(onehot, axis=0) - onehot) * onehot, axis=1)
    target = destination * capacity + leaf_rank
    payload = jnp.concatenate([positions, masses[:, None, :]], axis=1)
    placing = (jnp.arange(slot_count, dtype=jnp.int32)[:, None] == target[None, :]).astype(jnp.float32)
    outgoing = jnp.dot(
        placing, payload.reshape(leaves, -1), precision=exact, preferred_element_type=jnp.float32
    ).reshape(slot_count, 4, leaf_width)
    quarters = GSPAN // GROUP_DEV
    first_sums = local_sums(jnp.concatenate([mass_flat[None, :], mass_flat[None, :] * speeds], axis=0))
    table_size = capacity * 4 * leaf_width
    packed = jnp.concatenate(
        [outgoing.reshape(owners, table_size), jnp.broadcast_to(first_sums.reshape(1, -1), (owners, first_sums.size))],
        axis=1,
    )
    packed = lax.all_to_all(packed, "grp", split_axis=0, concat_axis=0, tiled=True)
    owned = packed[:, :table_size].reshape(slot_count, 4, leaf_width)
    row_sums = packed[:, table_size:].reshape((owners,) + first_sums.shape)

    per_peer = send_list.shape[2]
    pick = boundary_set[0].at[send_list[0]].get(mode="promise_in_bounds")
    live = jnp.arange(per_peer, dtype=jnp.int32)[None, :] < send_count[0][:, None]
    sending = owned.at[pick].get(mode="promise_in_bounds")
    sending = jnp.where(live[:, :, None, None], sending, jnp.zeros_like(sending))
    blocks = lax.axis_size("dom") * owners
    remote = lax.all_to_all(sending, "grp", split_axis=0, concat_axis=0, tiled=True)
    remote = remote.reshape(owners * per_peer, 4, leaf_width)
    domains = lax.axis_size("dom")
    before = lax.ppermute(row_sums, "dom", [(i, (i + 1) % domains) for i in range(domains)])
    after = lax.ppermute(row_sums, "dom", [(i, (i - 1) % domains) for i in range(domains)])
    three_rows = jnp.concatenate([before, row_sums, after], axis=0)
    span = 2 * quarters - 1
    window = lax.dynamic_slice_in_dim(three_rows, owners + lax.axis_index("grp") - (quarters - 1), span, axis=0)
    near_sums = {step: window[step + quarters - 1] for step in range(-quarters + 1, quarters)}

    near_parts = []
    for ahead in range(quarters):
        part = 0.0
        for back in range(quarters):
            part = part + near_sums[ahead - back][:, back * GROUP_DEV:(back + 1) * GROUP_DEV]
        near_parts.append(part)
    near = jnp.concatenate(near_parts, axis=1)
    bulk_local = near[1:] / near[0:1]
    per_particle = jnp.dot(bulk_local, member, precision=exact, preferred_element_type=jnp.float32)
    relative = speeds - per_particle
    kinetic = 0.5 * jnp.sum(relative * relative, axis=0)
    heat_local = local_sums((mass_flat * kinetic)[None, :])[0]
    partial = jnp.stack([heat_local, first_sums[0]])
    partial, remote = lax.optimization_barrier((partial, remote))
    combined = jnp.concatenate([owned, remote], axis=0)
    down = jnp.broadcast_to(partial[None], (domains,) + partial.shape)
    down = lax.all_to_all(down, "dom", split_axis=0, concat_axis=0, tiled=True)

    coupling = 1.0 / (partners.shape[1] * leaf_width)
    halves = []
    half = slot_count // 2
    for part in range(2):
        rows = partners[part * half:(part + 1) * half]
        sources = combined.at[rows].get(mode="promise_in_bounds")
        halves.append(tile_potential(owned[part * half:(part + 1) * half], sources))
    potential = jnp.concatenate(halves, axis=0) * coupling
    flat = potential.reshape(owners, capacity * leaf_width)
    extra = jnp.broadcast_to(down.reshape(1, -1), (owners, down.size))
    back = lax.all_to_all(jnp.concatenate([flat, extra], axis=1), "grp", split_axis=0, concat_axis=0, tiled=True)
    returned = back[:, :capacity * leaf_width].reshape(slot_count, leaf_width)
    every = back[:, capacity * leaf_width:].reshape((owners, domains) + partial.shape)
    every = jnp.transpose(every, (1, 0, 2, 3)).reshape(blocks, 2, quarters, GROUP_DEV)
    totals = every[:, :, 0, :]
    for shift in range(1, quarters):
        totals = totals + jnp.roll(every[:, :, shift, :], shift, axis=0)
    group_kinetic = totals[:, 0, :].reshape(groups) / totals[:, 1, :].reshape(groups)
    own_potential = returned.at[target].get(mode="promise_in_bounds")
    energy = kinetic.reshape(leaves, leaf_width) + own_potential
    return (energy, group_kinetic)


def solution(mesh):
    in_specs = (
        P(("dom", "grp"), None, None),
        P(("dom", "grp"), None, None),
        P(("dom", "grp"), None),
        P(("dom", "grp")),
        P(("dom", "grp"), None),
        P(("dom", "grp"), None),
        P(("dom", "grp"), None, None),
        P(("dom", "grp"), None),
        P(("dom", "grp"), None),
    )
    out_specs = (P(("dom", "grp"), None), P())
    return jax.shard_map(layer, mesh=mesh, in_specs=in_specs, out_specs=out_specs, check_vma=False)
```

```python
import jax
import jax.numpy as jnp
from jax import lax
from jax.sharding import PartitionSpec as P

GSPAN = 16
GROUP_DEV = 4


softening = 0.0025
exact = lax.Precision.HIGHEST


def tile_potential(targets, sources):
    distance = softening
    for component in range(3):
        offset = targets[:, None, component, :, None] - sources[:, :, component, None, :]
        distance = distance + offset * offset
    weights = sources[:, :, 3, None, :] * lax.rsqrt(distance)
    return -jnp.sum(weights, axis=(1, 3))


def layer(
    positions,
    velocities,
    masses,
    destination,
    group_ids,
    boundary_set,
    send_list,
    send_count,
    partners,
):
    owners = lax.axis_size("grp")
    leaves = positions.shape[0]
    leaf_width = positions.shape[2]
    capacity = 2 * leaves // owners
    slot_count = owners * capacity
    groups = GROUP_DEV * lax.axis_size("dom") * owners
    block_index = lax.axis_index("dom") * owners + lax.axis_index("grp")
    first_group = block_index * GROUP_DEV
    mass_flat = masses.reshape(-1)
    group_flat = group_ids.reshape(-1)
    speeds = jnp.transpose(velocities, (1, 0, 2)).reshape(3, -1)
    local_ids = (group_flat - first_group) % groups
    member = (jnp.arange(GSPAN, dtype=jnp.int32)[:, None] == local_ids[None, :]).astype(jnp.float32)

    def local_sums(stats):
        return jnp.einsum(
            "kp,gp->kg", stats, member, precision=exact, preferred_element_type=jnp.float32
        )

    onehot = (destination[:, None] == jnp.arange(owners, dtype=jnp.int32)[None, :]).astype(jnp.int32)
    leaf_rank = jnp.sum((jnp.cumsum(onehot, axis=0) - onehot) * onehot, axis=1)
    target = destination * capacity + leaf_rank
    payload = jnp.concatenate([positions, masses[:, None, :]], axis=1)
    holder = jnp.full((slot_count,), leaves, jnp.int32).at[target].set(jnp.arange(leaves, dtype=jnp.int32))
    outgoing = payload.at[holder].get(mode="fill", fill_value=0.0)
    owned = lax.all_to_all(outgoing, "grp", split_axis=0, concat_axis=0, tiled=True)

    per_peer = send_list.shape[2]
    pick = boundary_set[0].at[send_list[0]].get(mode="promise_in_bounds")
    live = jnp.arange(per_peer, dtype=jnp.int32)[None, :] < send_count[0][:, None]
    sending = owned.at[pick].get(mode="promise_in_bounds")
    sending = jnp.where(live[:, :, None, None], sending, jnp.zeros_like(sending))
    blocks = lax.axis_size("dom") * owners
    quarters = GSPAN // GROUP_DEV
    first_sums = local_sums(jnp.concatenate([mass_flat[None, :], mass_flat[None, :] * speeds], axis=0))
    leaf_size = per_peer * 4 * leaf_width
    packed = jnp.concatenate(
        [sending.reshape(owners, leaf_size), jnp.broadcast_to(first_sums.reshape(1, -1), (owners, first_sums.size))],
        axis=1,
    )
    packed = lax.all_to_all(packed, "grp", split_axis=0, concat_axis=0, tiled=True)
    remote = packed[:, :leaf_size].reshape(owners * per_peer, 4, leaf_width)
    row_sums = packed[:, leaf_size:].reshape((owners,) + first_sums.shape)
    domains = lax.axis_size("dom")
    before = lax.ppermute(row_sums, "dom", [(i, (i + 1) % domains) for i in range(domains)])
    after = lax.ppermute(row_sums, "dom", [(i, (i - 1) % domains) for i in range(domains)])
    three_rows = jnp.concatenate([before, row_sums, after], axis=0)
    span = 2 * quarters - 1
    window = lax.dynamic_slice_in_dim(three_rows, owners + lax.axis_index("grp") - (quarters - 1), span, axis=0)
    near_sums = {step: window[step + quarters - 1] for step in range(-quarters + 1, quarters)}
    combined = jnp.concatenate([owned, remote], axis=0)

    near_parts = []
    for ahead in range(quarters):
        part = 0.0
        for back in range(quarters):
            part = part + near_sums[ahead - back][:, back * GROUP_DEV:(back + 1) * GROUP_DEV]
        near_parts.append(part)
    near = jnp.concatenate(near_parts, axis=1)
    bulk_local = near[1:] / near[0:1]
    per_particle = jnp.dot(bulk_local, member, precision=exact, preferred_element_type=jnp.float32)
    relative = speeds - per_particle
    kinetic = 0.5 * jnp.sum(relative * relative, axis=0)
    heat_local = local_sums((mass_flat * kinetic)[None, :])[0]
    partial = jnp.stack([heat_local, first_sums[0]])
    down = jnp.broadcast_to(partial[None], (domains,) + partial.shape)
    down = lax.all_to_all(down, "dom", split_axis=0, concat_axis=0, tiled=True)

    coupling = 1.0 / (partners.shape[1] * leaf_width)
    halves = []
    half = slot_count // 2
    for part in range(2):
        rows = partners[part * half:(part + 1) * half]
        sources = combined.at[rows].get(mode="promise_in_bounds")
        halves.append(tile_potential(owned[part * half:(part + 1) * half], sources))
    potential = jnp.concatenate(halves, axis=0) * coupling
    flat = potential.reshape(owners, capacity * leaf_width)
    extra = jnp.broadcast_to(down.reshape(1, -1), (owners, down.size))
    back = lax.all_to_all(jnp.concatenate([flat, extra], axis=1), "grp", split_axis=0, concat_axis=0, tiled=True)
    returned = back[:, :capacity * leaf_width].reshape(slot_count, leaf_width)
    every = back[:, capacity * leaf_width:].reshape((owners, domains) + partial.shape)
    every = jnp.transpose(every, (1, 0, 2, 3)).reshape(blocks, 2, quarters, GROUP_DEV)
    totals = every[:, :, 0, :]
    for shift in range(1, quarters):
        totals = totals + jnp.roll(every[:, :, shift, :], shift, axis=0)
    group_kinetic = totals[:, 0, :].reshape(groups) / totals[:, 1, :].reshape(groups)
    own_potential = returned.at[target].get(mode="promise_in_bounds")
    energy = kinetic.reshape(leaves, leaf_width) + own_potential
    return (energy, group_kinetic)


def solution(mesh):
    in_specs = (
        P(("dom", "grp"), None, None),
        P(("dom", "grp"), None, None),
        P(("dom", "grp"), None),
        P(("dom", "grp")),
        P(("dom", "grp"), None),
        P(("dom", "grp"), None),
        P(("dom", "grp"), None, None),
        P(("dom", "grp"), None),
        P(("dom", "grp"), None),
    )
    out_specs = (P(("dom", "grp"), None), P())
    return jax.shard_map(layer, mesh=mesh, in_specs=in_specs, out_specs=out_specs, check_vma=False)
```
